256 devices in a mesh: dp: 32 (over z, x_hi, core), tm: 8 (over y, x_lo).
Axes of the slice: x: 4 (x_hi: 2, x_lo: 2; x = x_hi * 2 + x_lo), y: 4, z: 8, core: 2. Of those that a mesh axis runs over, the one named last changes fastest.
Arguments:
- queries: bfloat16 [32, 3072, 256], P('dp', 'tm'), may hold values from -6 to 6
- key_input: bfloat16 [32, 3072, 256], P('dp', 'tm'), may hold values from -6 to 6
- value_input: bfloat16 [32, 3072, 256], P('dp', 'tm'), may hold values from -6 to 6
- lengths: int32 [32], P('dp'), may hold values from 1536 to 3072, as said below
- projection: bfloat16 [4096, 256], P('dp'), may hold values from -0.09375 to 0.09375
- upstream: bfloat16 [32, 3072, 4096], P('dp', 'tm'), may hold values from -6 to 6
- glu_input: bfloat16 [32, 3072, 4096], P('dp', 'tm'), may hold values from -6 to 6
- kernel: bfloat16 [2048, 31], P('dp'), may hold values from -1 to 1
- norm_gain: bfloat16 [2048], P('dp'), may hold values from 0.5 to 1.5
- conv_upstream: bfloat16 [32, 3072, 2048], P('dp', 'tm'), may hold values from -6 to 6
Outputs:
- grad_queries: bfloat16 [32, 3072, 256], P('dp', 'tm')
- grad_keys: bfloat16 [32, 3072, 256], P('dp', 'tm')
- grad_values: bfloat16 [32, 3072, 256], P('dp', 'tm')
- grad_projection: bfloat16 [4096, 256], P('dp')
- grad_glu: bfloat16 [32, 3072, 4096], P('dp', 'tm')
- grad_kernel: float32 [2048, 31], P('dp')
- grad_gain: float32 [2048], P('dp')
The draws below stay inside these ranges and needn't reach their ends.
Inputs may be any that keep to these rules, and one draw needn't show every extreme that they name: `lengths`: the valid frames of an utterance are its first ones; one utterance has all 3072 valid and one exactly 1536.
All inputs are finite; a program needn't handle non-finite values.
Results may differ from the reference program's by a relative error of at most 0.02.
Values may be sent and summed in bfloat16 or wider, within the bound.
No kernel may reach another device: no remote copies, remote signals or barrier semaphores. Data moves between devices by JAX's collectives and lax.ppermute only.
A program may use at most 128 MiB of HBM per device.

```python
import jax
import jax.numpy as jnp
from jax import lax

D = 4096
HEADS = 2
HDIM = 128
CH = 2048
KW = 31
UTTS = 32
FRAMES = 3072


def query_key_pair(key):
    base = jax.random.fold_in(key, 11)
    first, second = jax.random.split(base, 2)
    shape = (UTTS, FRAMES, HEADS * HDIM)
    query_vals = jnp.clip(jax.random.normal(first, shape, jnp.float32), -6.0, 6.0)
    key_vals = jnp.clip(jax.random.normal(second, shape, jnp.float32), -6.0, 6.0)
    return (query_vals, key_vals)


def draw_queries(key, part):
    return query_key_pair(key)[0].astype(jnp.bfloat16)


def draw_key_input(key, part):
    return query_key_pair(key)[1].astype(jnp.bfloat16)


def draw_lengths(key, part):
    base = jax.random.fold_in(key, 23)
    first, second, third = jax.random.split(base, 3)
    drawn = jax.random.randint(first, (UTTS,), FRAMES // 2, FRAMES + 1)
    longest = jax.random.randint(second, (), 0, UTTS)
    shortest = (longest + 1 + jax.random.randint(third, (), 0, UTTS - 1)) % UTTS
    return drawn.at[longest].set(FRAMES).at[shortest].set(FRAMES // 2).astype(jnp.int32)


def strengthened(values, own_key, source, target, shards_of, factor):
    def block_of(axis_at):
        return (jnp.arange(values.shape[axis_at]) // (values.shape[axis_at] // shards_of)).reshape((-1,) + (1,) * (values.ndim - 1 - axis_at))

    near = jax.random.permutation(own_key, shards_of)[block_of(target)]
    other_side = (block_of(target) + shards_of // 2) % shards_of
    return jnp.where((block_of(source) == near) | (block_of(source) == other_side), factor * values, values)


def block_levels(own_key, dims, cuts, least, largest):
    def one(dim, shards_of):
        steps = jax.random.uniform(jax.random.fold_in(jax.random.fold_in(own_key, 6), dim), (shards_of,), jnp.float32, least / len(cuts), largest / len(cuts))
        return jnp.repeat(jnp.exp(steps), dims[dim] // shards_of).reshape((-1,) + (1,) * (len(dims) - dim - 1))

    gain = one(*cuts[0])
    for cut in cuts[1:]:
        gain = gain * one(*cut)
    return gain


def scatter_about(stream_key, dims, deviation, reach, shards=(), held_as=jnp.bfloat16):
    loudness = block_levels(stream_key, dims, shards, -0.22, 0.18) if shards else 1.0
    entries = jax.random.normal(stream_key, dims, jnp.float32) * deviation * loudness
    return jnp.minimum(jnp.maximum(entries, -reach), reach).astype(held_as)


def bell_draw_with(rng, shape, width, bound, cuts, heavy, kind=jnp.bfloat16):
    values = width * jax.random.normal(rng, shape, jnp.float32)
    if cuts:
        values = values * block_levels(rng, shape, cuts, -0.22, 0.18)
    return jnp.clip(strengthened(values, jax.random.fold_in(rng, 3), *heavy), -bound, bound).astype(kind)


def setup_inputs(seed: int = 0) -> dict:
    streams_of = jax.random.split(jax.random.key(seed), 11)
    queries = draw_queries(jax.random.fold_in(streams_of[10], 71), 0)
    key_input = draw_key_input(jax.random.fold_in(streams_of[10], 71), 0)
    value_input = scatter_about(streams_of[2], (UTTS, FRAMES, HEADS * HDIM), 1.0, 6.0, ((0, 32), (1, 8)))
    lengths = draw_lengths(jax.random.fold_in(streams_of[10], 71), 0)
    projection = scatter_about(streams_of[4], (D, HEADS * HDIM), D ** -0.5, 0.09375, ((0, 32),))
    upstream = bell_draw_with(streams_of[5], (UTTS, FRAMES, D), 1.0, 6.0, ((0, 32), (1, 8)), (0, 2, 32, 2.75))
    glu_input = scatter_about(streams_of[6], (UTTS, FRAMES, 2 * CH), 1.0, 6.0, ((0, 32), (1, 8)))
    kernel = scatter_about(streams_of[7], (CH, KW), KW ** -0.5, 1.0, ((0, 32),))
    norm_gain = jnp.clip(1.0 + 0.1 * jax.random.normal(streams_of[8], (CH,), jnp.float32), 0.5, 1.5).astype(jnp.bfloat16)
    conv_upstream = bell_draw_with(streams_of[9], (UTTS, FRAMES, CH), 1.0, 6.0, ((0, 32), (1, 8)), (0, 2, 32, 2.75))
    return {"queries": queries, "key_input": key_input, "value_input": value_input, "lengths": lengths, "projection": projection, "upstream": upstream, "glu_input": glu_input, "kernel": kernel, "norm_gain": norm_gain, "conv_upstream": conv_upstream}


NEG_FILL = -1e+30
NORM_EPS = 1e-05

def settle(values):
    return lax.optimization_barrier(values)

def depthwise(padded, kernel_f, frame_rows):
    mixed = jnp.zeros((frame_rows, kernel_f.shape[0]), jnp.float32)
    for tap in range(kernel_f.shape[1]):
        mixed = mixed + padded[tap:tap + frame_rows].astype(jnp.float32) * kernel_f[:, tap]
    return mixed

def back_depthwise(grad_pad, kernel_f, frame_rows):
    half_width = (kernel_f.shape[1] - 1) // 2
    result = jnp.zeros((frame_rows, kernel_f.shape[0]), jnp.float32)
    for tap in range(kernel_f.shape[1]):
        begin = 2 * half_width - tap
        result = result + grad_pad[begin:begin + frame_rows].astype(jnp.float32) * kernel_f[:, tap]
    return result

def tap_products(grad_low, padded, frame_rows, tap_count):
    grad_f = grad_low.astype(jnp.float32)
    return jnp.stack([lax.optimization_barrier(jnp.sum(grad_f * padded[tap:tap + frame_rows].astype(jnp.float32), axis=0)) for tap in range(tap_count)], axis=1)

def norm_backward(mixed, gain_f, cotangent, frame_live):
    centre = mixed - lax.optimization_barrier(jnp.mean(mixed, axis=-1, keepdims=True))
    inv_std = lax.rsqrt(lax.optimization_barrier(jnp.mean(centre * centre, axis=-1, keepdims=True)) + NORM_EPS)
    standard = centre * inv_std
    normed = standard * gain_f
    squash = jax.nn.sigmoid(normed)
    grad_normed = cotangent.astype(jnp.float32) * frame_live * (squash + normed * squash * (1.0 - squash))
    gain_term = lax.optimization_barrier(jnp.sum(grad_normed * standard, axis=0))
    scaled = grad_normed * gain_f
    grad_conv = inv_std * (scaled - lax.optimization_barrier(jnp.mean(scaled, axis=-1, keepdims=True)) - standard * lax.optimization_barrier(jnp.mean(scaled * standard, axis=-1, keepdims=True)))
    return (grad_conv.astype(jnp.bfloat16), gain_term)

def attention_grads(query_utt, key_utt, value_utt, upstream_utt, length, projection):
    score_scale = HDIM ** (-0.5)
    query_heads = query_utt.reshape(FRAMES, HEADS, HDIM).astype(jnp.float32)
    key_heads = key_utt.reshape(FRAMES, HEADS, HDIM).astype(jnp.float32)
    value_heads = value_utt.reshape(FRAMES, HEADS, HDIM).astype(jnp.float32)
    scores = jnp.einsum('qhd,khd->hqk', query_heads, key_heads, precision=lax.Precision.HIGHEST) * score_scale
    key_live = jnp.arange(FRAMES, dtype=jnp.int32) < length
    scores = jnp.where(key_live[None, None, :], scores, NEG_FILL)
    row_top = lax.optimization_barrier(jnp.max(scores, axis=-1, keepdims=True))
    log_total = row_top + jnp.log(lax.optimization_barrier(jnp.sum(jnp.exp(scores - row_top), axis=-1, keepdims=True)))
    weights = jnp.exp(scores - log_total)
    weights_low = settle(weights.astype(jnp.bfloat16)).astype(jnp.float32)
    attended = jnp.einsum('hqk,khd->qhd', weights, value_heads, precision=lax.Precision.HIGHEST).astype(jnp.bfloat16)
    grad_out = jnp.dot(upstream_utt, projection, preferred_element_type=jnp.float32).astype(jnp.bfloat16)
    grad_heads = grad_out.reshape(FRAMES, HEADS, HDIM).astype(jnp.float32)
    attended_f = attended.astype(jnp.float32)
    row_delta = jnp.einsum('qhd,qhd->hq', grad_heads, attended_f, precision=lax.Precision.HIGHEST)
    grad_value = jnp.einsum('hqk,qhd->khd', weights_low, grad_heads, precision=lax.Precision.HIGHEST)
    grad_weights = jnp.einsum('qhd,khd->hqk', grad_heads, value_heads, precision=lax.Precision.HIGHEST)
    grad_scores = (weights * (grad_weights - row_delta[:, :, None]) * score_scale).astype(jnp.bfloat16)
    grad_scores = settle(grad_scores).astype(jnp.float32)
    grad_query = jnp.einsum('hqk,khd->qhd', grad_scores, key_heads, precision=lax.Precision.HIGHEST)
    grad_key = jnp.einsum('hqk,qhd->khd', grad_scores, query_heads, precision=lax.Precision.HIGHEST)
    attended_flat = attended.reshape(FRAMES, HEADS * HDIM)
    proj_term = lax.dot_general(upstream_utt, attended_flat, (((0,), (0,)), ((), ())), preferred_element_type=jnp.float32)
    flat_width = HEADS * HDIM
    return (grad_query.reshape(FRAMES, flat_width).astype(jnp.bfloat16), grad_key.reshape(FRAMES, flat_width).astype(jnp.bfloat16), grad_value.reshape(FRAMES, flat_width).astype(jnp.bfloat16), proj_term)

def conv_grads(glu_utt, cot_utt, length, kernel_f, gain_f):
    half_width = (KW - 1) // 2
    frame_ids = jnp.arange(FRAMES, dtype=jnp.int32)
    frame_live = (frame_ids < length).astype(jnp.float32)[:, None]
    linear = glu_utt[:, :CH].astype(jnp.float32)
    gate_sig = jax.nn.sigmoid(glu_utt[:, CH:].astype(jnp.float32))
    activ = (linear * gate_sig * frame_live).astype(jnp.bfloat16)
    padded = jnp.pad(activ, ((half_width, half_width), (0, 0)))
    mixed = depthwise(padded, kernel_f, FRAMES)
    grad_conv, gain_term = norm_backward(mixed, gain_f, cot_utt, frame_live)
    grad_pad = jnp.pad(grad_conv, ((half_width, half_width), (0, 0)))
    kernel_term = tap_products(grad_conv, padded, FRAMES, KW)
    grad_activ = back_depthwise(grad_pad, kernel_f, FRAMES) * frame_live
    first_half = grad_activ * gate_sig
    second_half = grad_activ * linear * gate_sig * (1.0 - gate_sig)
    grad_glu = jnp.concatenate([first_half, second_half], axis=-1).astype(jnp.bfloat16)
    return (grad_glu, kernel_term, gain_term)

def reference(queries, key_input, value_input, lengths, projection, upstream, glu_input, kernel, norm_gain, conv_upstream):
    kernel_f = kernel.astype(jnp.float32)
    gain_f = norm_gain.astype(jnp.float32)

    def per_utterance(totals, items):
        query_utt, key_utt, value_utt, upstream_utt, glu_utt, cot_utt, length = items
        grad_query, grad_key, grad_value, proj_term = attention_grads(query_utt, key_utt, value_utt, upstream_utt, length, projection)
        grad_glu, kernel_term, gain_term = conv_grads(glu_utt, cot_utt, length, kernel_f, gain_f)
        totals = (totals[0] + proj_term, totals[1] + kernel_term, totals[2] + gain_term)
        return (totals, (grad_query, grad_key, grad_value, grad_glu))
    start_totals = (jnp.zeros((D, HEADS * HDIM), jnp.float32), jnp.zeros((CH, KW), jnp.float32), jnp.zeros((CH,), jnp.float32))
    totals, stacked = lax.scan(per_utterance, start_totals, (queries, key_input, value_input, upstream, glu_input, conv_upstream, lengths))
    return (stacked[0], stacked[1], stacked[2], totals[0].astype(jnp.bfloat16), stacked[3], totals[1], totals[2])
```

```python
import jax
import jax.numpy as jnp
from jax import lax
from jax.sharding import PartitionSpec as P

HEADS = 2
HDIM = 128
CH = 2048
KW = 31


NEG_FILL = -1e30
NORM_EPS = 1e-05


def from_behind(block, axis, distance):
    devices = range(lax.axis_size(axis))
    route = [((i - distance) % len(devices), i) for i in devices]
    return lax.ppermute(block, axis, route)


def extended(cells, sides, width):
    for axis, dim in sides:
        count = lax.axis_size(axis)
        ends = count - 1
        head = lax.slice_in_dim(cells, 0, width, axis=dim)
        tail = lax.slice_in_dim(cells, cells.shape[dim] - width, cells.shape[dim], axis=dim)
        cells = jnp.concatenate(
            [
                lax.ppermute(tail, axis, [(i, (i + 1) % count) for i in range(ends)]),
                cells,
                lax.ppermute(head, axis, [((i + 1) % count, i) for i in range(ends)]),
            ],
            axis=dim,
        )
    return cells


def depthwise(padded, kernel_f, frame_rows):
    mixed = jnp.zeros((frame_rows, kernel_f.shape[0]), jnp.float32)
    for tap in range(kernel_f.shape[1]):
        mixed = mixed + padded[tap : tap + frame_rows].astype(jnp.float32) * kernel_f[:, tap]
    return mixed


def back_depthwise(grad_pad, kernel_f, frame_rows):
    half_width = (kernel_f.shape[1] - 1) // 2
    result = jnp.zeros((frame_rows, kernel_f.shape[0]), jnp.float32)
    for tap in range(kernel_f.shape[1]):
        begin = 2 * half_width - tap
        result = (
            result + grad_pad[begin : begin + frame_rows].astype(jnp.float32) * kernel_f[:, tap]
        )
    return result


def tap_products(grad_low, padded, frame_rows, tap_count):
    grad_f = grad_low.astype(jnp.float32)
    return jnp.stack(
        [
            jnp.sum(grad_f * padded[tap : tap + frame_rows].astype(jnp.float32), axis=0)
            for tap in range(tap_count)
        ],
        axis=1,
    )


def norm_backward(mixed, gain_f, cotangent, frame_live):
    centre = mixed - jnp.mean(mixed, axis=-1, keepdims=True)
    inv_std = lax.rsqrt(jnp.mean(centre * centre, axis=-1, keepdims=True) + NORM_EPS)
    standard = centre * inv_std
    normed = standard * gain_f
    squash = jax.nn.sigmoid(normed)
    grad_normed = (
        cotangent.astype(jnp.float32) * frame_live * (squash + normed * squash * (1.0 - squash))
    )
    gain_term = jnp.sum(grad_normed * standard, axis=0)
    scaled = grad_normed * gain_f
    grad_conv = inv_std * (
        scaled
        - jnp.mean(scaled, axis=-1, keepdims=True)
        - standard * jnp.mean(scaled * standard, axis=-1, keepdims=True)
    )
    return (grad_conv.astype(jnp.bfloat16), gain_term)


def gather_params(projection, kernel, norm_gain):
    width = projection.shape[1]
    tail = jnp.concatenate([kernel.reshape(-1), norm_gain.reshape(-1)])
    tail_rows = -(-tail.shape[0] // width)
    tail = jnp.pad(tail, (0, tail_rows * width - tail.shape[0])).reshape(tail_rows, width)
    block = jnp.concatenate([projection, tail], axis=0)
    full = lax.all_gather(block, "dp", axis=0, tiled=False)
    count = full.shape[0]
    proj_rows = projection.shape[0]
    full_proj = full[:, :proj_rows].reshape(count * proj_rows, width)
    flat_tail = full[:, proj_rows:].reshape(count, tail_rows * width)
    kernel_size = kernel.shape[0] * kernel.shape[1]
    full_kernel = flat_tail[:, :kernel_size].reshape(count * kernel.shape[0], kernel.shape[1])
    full_gain = flat_tail[:, kernel_size : kernel_size + norm_gain.shape[0]].reshape(-1)
    return full_proj, full_kernel, full_gain


def reduce_grads(proj_term, kernel_term, gain_term):
    count = lax.axis_size("dp")
    width = proj_term.shape[1]
    proj_blocks = proj_term.reshape(count, -1, width)
    proj_rows = proj_blocks.shape[1]
    kernel_blocks = kernel_term.reshape(count, -1)
    gain_blocks = gain_term.reshape(count, -1)
    tail = jnp.concatenate([kernel_blocks, gain_blocks], axis=1)
    tail_cols = tail.shape[1]
    tail_rows = -(-tail_cols // width)
    tail = jnp.pad(tail, ((0, 0), (0, tail_rows * width - tail_cols))).reshape(
        count, tail_rows, width
    )
    packed = jnp.concatenate([proj_blocks, tail], axis=1).reshape(-1, width)
    part = lax.psum_scatter(packed, "dp", scatter_dimension=0, tiled=True)
    total = lax.psum(part, "tm")
    proj_total = total[:proj_rows]
    flat_tail = total[proj_rows:].reshape(-1)
    kernel_size = kernel_blocks.shape[1]
    kernel_total = flat_tail[:kernel_size].reshape(-1, kernel_term.shape[1])
    gain_total = flat_tail[kernel_size : kernel_size + gain_blocks.shape[1]]
    return proj_total, kernel_total, gain_total


def per_device(
    queries,
    key_input,
    value_input,
    lengths,
    projection,
    upstream,
    glu_input,
    kernel,
    norm_gain,
    conv_upstream,
):
    time_count = lax.axis_size("tm")
    time_rank = lax.axis_index("tm")
    frame_rows = queries.shape[1]
    flat_width = queries.shape[2]
    score_scale = HDIM ** (-0.5)
    length = lengths[0]
    full_proj, full_kernel, full_gain = gather_params(projection, kernel, norm_gain)
    query_heads = queries[0].reshape(frame_rows, HEADS, HDIM)
    key_heads = key_input[0].reshape(frame_rows, HEADS, HDIM)
    value_heads = value_input[0].reshape(frame_rows, HEADS, HDIM)

    def block_scores(key_block, key_offset):
        scores = (
            jnp.einsum("qhd,khd->hqk", query_heads, key_block, preferred_element_type=jnp.float32)
            * score_scale
        )
        key_live = key_offset + jnp.arange(key_block.shape[0], dtype=jnp.int32) < length
        return jnp.where(key_live[None, None, :], scores, NEG_FILL)

    def absorb(state_now, key_block, value_block, key_offset):
        run_top, run_total, run_acc = state_now
        scores = block_scores(key_block, key_offset)
        new_top = jnp.maximum(run_top, jnp.max(scores, axis=-1))
        factor = jnp.exp(run_top - new_top)
        weights = jnp.exp(scores - new_top[:, :, None])
        run_total = run_total * factor + jnp.sum(weights, axis=-1)
        contrib = jnp.einsum(
            "hqk,khd->qhd",
            weights,
            value_block.astype(jnp.float32),
            precision=lax.Precision.HIGHEST,
        )
        run_acc = run_acc * jnp.transpose(factor)[:, :, None] + contrib
        return (new_top, run_total, run_acc)

    start_state = (
        jnp.full((HEADS, frame_rows), NEG_FILL, jnp.float32),
        jnp.zeros((HEADS, frame_rows), jnp.float32),
        jnp.zeros((frame_rows, HEADS, HDIM), jnp.float32),
    )

    def forward_step(step, loop_state):
        key_block, value_block, inner = loop_state
        source = (time_rank - step) % time_count
        inner = absorb(inner, key_block, value_block, source * frame_rows)
        key_block, value_block = from_behind((key_block, value_block), "tm", 1)
        return (key_block, value_block, inner)

    key_block, value_block, inner = lax.fori_loop(
        0, time_count - 1, forward_step, (key_heads, value_heads, start_state)
    )
    source = (time_rank - (time_count - 1)) % time_count
    state_now = absorb(inner, key_block, value_block, source * frame_rows)
    run_top, run_total, run_acc = state_now
    log_total = run_top + jnp.log(run_total)
    attended = (run_acc / jnp.transpose(run_total)[:, :, None]).astype(jnp.bfloat16)
    upstream_rows = upstream[0]
    grad_out = jnp.dot(upstream_rows, full_proj, preferred_element_type=jnp.float32).astype(
        jnp.bfloat16
    )
    grad_heads = grad_out.reshape(frame_rows, HEADS, HDIM)
    row_delta = jnp.einsum("qhd,qhd->hq", grad_heads, attended, preferred_element_type=jnp.float32)

    def backward_block(key_block, value_block, key_offset):
        scores = block_scores(key_block, key_offset)
        weights = jnp.exp(scores - log_total[:, :, None])
        weights_low = weights.astype(jnp.bfloat16)
        add_value = jnp.einsum(
            "hqk,qhd->khd", weights_low, grad_heads, preferred_element_type=jnp.float32
        )
        grad_weights = jnp.einsum(
            "qhd,khd->hqk", grad_heads, value_block, preferred_element_type=jnp.float32
        )
        grad_scores = (weights * (grad_weights - row_delta[:, :, None]) * score_scale).astype(
            jnp.bfloat16
        )
        add_query = jnp.einsum(
            "hqk,khd->qhd", grad_scores, key_block, preferred_element_type=jnp.float32
        )
        add_key = jnp.einsum(
            "hqk,qhd->khd", grad_scores, query_heads, preferred_element_type=jnp.float32
        )
        return (add_query, add_key, add_value)

    zero_heads = jnp.zeros((frame_rows, HEADS, HDIM), jnp.float32)

    def pass_grads(key_acc, value_acc):
        return from_behind((key_acc, value_acc), "tm", 1)

    def backward_step(step, loop_state):
        key_block, value_block, key_acc, value_acc, query_acc = loop_state
        source = (time_rank - step) % time_count
        add_query, add_key, add_value = backward_block(key_block, value_block, source * frame_rows)
        key_acc, value_acc = pass_grads(key_acc + add_key, value_acc + add_value)
        key_block, value_block = from_behind((key_block, value_block), "tm", 1)
        return (key_block, value_block, key_acc, value_acc, query_acc + add_query)

    key_block, value_block, key_acc, value_acc, query_acc = lax.fori_loop(
        0,
        time_count - 1,
        backward_step,
        (key_heads, value_heads, zero_heads, zero_heads, zero_heads),
    )
    source = (time_rank - (time_count - 1)) % time_count
    add_query, add_key, add_value = backward_block(key_block, value_block, source * frame_rows)
    key_acc, value_acc = pass_grads(key_acc + add_key, value_acc + add_value)
    query_acc = query_acc + add_query
    grad_queries = query_acc.reshape(1, frame_rows, flat_width).astype(jnp.bfloat16)
    grad_keys = key_acc.reshape(1, frame_rows, flat_width).astype(jnp.bfloat16)
    grad_values = value_acc.reshape(1, frame_rows, flat_width).astype(jnp.bfloat16)
    half_width = (KW - 1) // 2
    frame_ids = time_rank * frame_rows + jnp.arange(frame_rows, dtype=jnp.int32)
    frame_live = (frame_ids < length).astype(jnp.float32)[:, None]
    glu_rows = glu_input[0]
    linear = glu_rows[:, :CH].astype(jnp.float32)
    gate_sig = jax.nn.sigmoid(glu_rows[:, CH:].astype(jnp.float32))
    activ = (linear * gate_sig * frame_live).astype(jnp.bfloat16)
    padded = extended(activ, (("tm", 0),), half_width)
    kernel_f = full_kernel.astype(jnp.float32)
    gain_f = full_gain.astype(jnp.float32)
    mixed = depthwise(padded, kernel_f, frame_rows)
    grad_conv, gain_term = norm_backward(mixed, gain_f, conv_upstream[0], frame_live)
    grad_pad = extended(grad_conv, (("tm", 0),), half_width)
    kernel_term = tap_products(grad_conv, padded, frame_rows, KW)
    grad_activ = back_depthwise(grad_pad, kernel_f, frame_rows) * frame_live
    first_half = grad_activ * gate_sig
    second_half = grad_activ * linear * gate_sig * (1.0 - gate_sig)
    grad_glu = jnp.concatenate([first_half, second_half], axis=-1).astype(jnp.bfloat16)[None]
    attended_flat = attended.reshape(frame_rows, flat_width)
    proj_term = lax.dot_general(
        upstream_rows,
        attended_flat,
        (((0,), (0,)), ((), ())),
        preferred_element_type=jnp.float32,
    )
    proj_total, kernel_total, gain_total = reduce_grads(proj_term, kernel_term, gain_term)
    grad_projection = proj_total.astype(jnp.bfloat16)
    return (
        grad_queries,
        grad_keys,
        grad_values,
        grad_projection,
        grad_glu,
        kernel_total,
        gain_total,
    )


def solution(mesh):
    in_specs = (
        P("dp", "tm", None),
        P("dp", "tm", None),
        P("dp", "tm", None),
        P("dp"),
        P("dp", None),
        P("dp", "tm", None),
        P("dp", "tm", None),
        P("dp", None),
        P("dp"),
        P("dp", "tm", None),
    )
    out_specs = (
        P("dp", "tm", None),
        P("dp", "tm", None),
        P("dp", "tm", None),
        P("dp", None),
        P("dp", "tm", None),
        P("dp", None),
        P("dp"),
    )
    return jax.shard_map(
        per_device, mesh=mesh, in_specs=in_specs, out_specs=out_specs, check_vma=False
    )
```

```python
import jax
import jax.numpy as jnp
from jax import lax
from jax.sharding import PartitionSpec as P

HEADS = 2
HDIM = 128
CH = 2048
KW = 31


NEG_FILL = -1e30
NORM_EPS = 1e-05


def from_behind(block, axis, distance):
    devices = range(lax.axis_size(axis))
    route = [((i - distance) % len(devices), i) for i in devices]
    return lax.ppermute(block, axis, route)


def extended(cells, sides, width):
    for axis, dim in sides:
        count = lax.axis_size(axis)
        ends = count - 1
        head = lax.slice_in_dim(cells, 0, width, axis=dim)
        tail = lax.slice_in_dim(cells, cells.shape[dim] - width, cells.shape[dim], axis=dim)
        cells = jnp.concatenate(
            [
                lax.ppermute(tail, axis, [(i, (i + 1) % count) for i in range(ends)]),
                cells,
                lax.ppermute(head, axis, [((i + 1) % count, i) for i in range(ends)]),
            ],
            axis=dim,
        )
    return cells


def depthwise(padded, kernel_f, frame_rows):
    mixed = jnp.zeros((frame_rows, kernel_f.shape[0]), jnp.float32)
    for tap in range(kernel_f.shape[1]):
        mixed = mixed + padded[tap : tap + frame_rows].astype(jnp.float32) * kernel_f[:, tap]
    return mixed


def back_depthwise(grad_pad, kernel_f, frame_rows):
    half_width = (kernel_f.shape[1] - 1) // 2
    result = jnp.zeros((frame_rows, kernel_f.shape[0]), jnp.float32)
    for tap in range(kernel_f.shape[1]):
        begin = 2 * half_width - tap
        result = (
            result + grad_pad[begin : begin + frame_rows].astype(jnp.float32) * kernel_f[:, tap]
        )
    return result


def tap_products(grad_low, padded, frame_rows, tap_count):
    grad_f = grad_low.astype(jnp.float32)
    return jnp.stack(
        [
            jnp.sum(grad_f * padded[tap : tap + frame_rows].astype(jnp.float32), axis=0)
            for tap in range(tap_count)
        ],
        axis=1,
    )


def norm_backward(mixed, gain_f, cotangent, frame_live):
    centre = mixed - jnp.mean(mixed, axis=-1, keepdims=True)
    inv_std = lax.rsqrt(jnp.mean(centre * centre, axis=-1, keepdims=True) + NORM_EPS)
    standard = centre * inv_std
    normed = standard * gain_f
    squash = jax.nn.sigmoid(normed)
    grad_normed = (
        cotangent.astype(jnp.float32) * frame_live * (squash + normed * squash * (1.0 - squash))
    )
    gain_term = jnp.sum(grad_normed * standard, axis=0)
    scaled = grad_normed * gain_f
    grad_conv = inv_std * (
        scaled
        - jnp.mean(scaled, axis=-1, keepdims=True)
        - standard * jnp.mean(scaled * standard, axis=-1, keepdims=True)
    )
    return (grad_conv.astype(jnp.bfloat16), gain_term)


def gather_params(projection, kernel, norm_gain):
    width = projection.shape[1]
    tail = jnp.concatenate([kernel.reshape(-1), norm_gain.reshape(-1)])
    tail_rows = -(-tail.shape[0] // width)
    tail = jnp.pad(tail, (0, tail_rows * width - tail.shape[0])).reshape(tail_rows, width)
    block = jnp.concatenate([projection, tail], axis=0)
    full = lax.all_gather(block, "dp", axis=0, tiled=False)
    count = full.shape[0]
    proj_rows = projection.shape[0]
    full_proj = full[:, :proj_rows].reshape(count * proj_rows, width)
    flat_tail = full[:, proj_rows:].reshape(count, tail_rows * width)
    kernel_size = kernel.shape[0] * kernel.shape[1]
    full_kernel = flat_tail[:, :kernel_size].reshape(count * kernel.shape[0], kernel.shape[1])
    full_gain = flat_tail[:, kernel_size : kernel_size + norm_gain.shape[0]].reshape(-1)
    return full_proj, full_kernel, full_gain


def reduce_grads(proj_term, kernel_term, gain_term):
    count = lax.axis_size("dp")
    width = proj_term.shape[1]
    proj_part = lax.psum_scatter(proj_term, "dp", scatter_dimension=0, tiled=True)
    kernel_blocks = kernel_term.reshape(count, -1)
    gain_blocks = gain_term.reshape(count, -1)
    tail = jnp.concatenate([kernel_blocks, gain_blocks], axis=1)
    tail_cols = tail.shape[1]
    tail_rows = -(-tail_cols // width)
    tail = jnp.pad(tail, ((0, 0), (0, tail_rows * width - tail_cols))).reshape(-1, width)
    tail_part = lax.psum_scatter(tail, "dp", scatter_dimension=0, tiled=True)
    total = lax.psum(jnp.concatenate([proj_part, tail_part], axis=0), "tm")
    proj_rows = proj_part.shape[0]
    proj_total = total[:proj_rows]
    flat_tail = total[proj_rows:].reshape(-1)
    kernel_size = kernel_blocks.shape[1]
    kernel_total = flat_tail[:kernel_size].reshape(-1, kernel_term.shape[1])
    gain_total = flat_tail[kernel_size : kernel_size + gain_blocks.shape[1]]
    return proj_total, kernel_total, gain_total


def split_three(values):
    high = lax.optimization_barrier(values.astype(jnp.bfloat16))
    rest = values - high.astype(jnp.float32)
    middle = lax.optimization_barrier(rest.astype(jnp.bfloat16))
    low = (rest - middle.astype(jnp.float32)).astype(jnp.bfloat16)
    return jnp.concatenate([high, middle, low], axis=0)


def join_three(parts):
    third = parts.shape[0] // 3
    wide = parts.astype(jnp.float32)
    return wide[:third] + wide[third : 2 * third] + wide[2 * third :]


def per_device(
    queries,
    key_input,
    value_input,
    lengths,
    projection,
    upstream,
    glu_input,
    kernel,
    norm_gain,
    conv_upstream,
):
    time_count = lax.axis_size("tm")
    time_rank = lax.axis_index("tm")
    frame_rows = queries.shape[1]
    flat_width = queries.shape[2]
    score_scale = HDIM ** (-0.5)
    length = lengths[0]
    full_proj, full_kernel, full_gain = gather_params(projection, kernel, norm_gain)
    query_heads = queries[0].reshape(frame_rows, HEADS, HDIM)
    key_own = key_input[0].reshape(frame_rows, HEADS, HDIM)
    value_own = value_input[0].reshape(frame_rows, HEADS, HDIM)
    key_value = lax.all_gather(
        jnp.concatenate([key_input[0], value_input[0]], axis=1), "tm", axis=0, tiled=True
    )
    total_frames = key_value.shape[0]
    key_all = key_value[:, :flat_width].reshape(total_frames, HEADS, HDIM)
    value_all = key_value[:, flat_width:].reshape(total_frames, HEADS, HDIM)
    key_live = jnp.arange(total_frames, dtype=jnp.int32) < length
    scores = (
        jnp.einsum("qhd,khd->hqk", query_heads, key_all, preferred_element_type=jnp.float32)
        * score_scale
    )
    scores = jnp.where(key_live[None, None, :], scores, NEG_FILL)
    row_top = jnp.max(scores, axis=-1)
    log_total = row_top + jnp.log(jnp.sum(jnp.exp(scores - row_top[:, :, None]), axis=-1))
    weights = jnp.exp(scores - log_total[:, :, None])
    weights_high = lax.optimization_barrier(weights.astype(jnp.bfloat16))
    weights_rest = (weights - weights_high.astype(jnp.float32)).astype(jnp.bfloat16)
    attended = (
        jnp.einsum("hqk,khd->qhd", weights_high, value_all, preferred_element_type=jnp.float32)
        + jnp.einsum("hqk,khd->qhd", weights_rest, value_all, preferred_element_type=jnp.float32)
    ).astype(jnp.bfloat16)
    upstream_rows = upstream[0]
    grad_out = jnp.dot(upstream_rows, full_proj, preferred_element_type=jnp.float32).astype(
        jnp.bfloat16
    )
    grad_heads = grad_out.reshape(frame_rows, HEADS, HDIM)
    row_delta = jnp.einsum("qhd,qhd->hq", grad_heads, attended, preferred_element_type=jnp.float32)
    grad_weights = jnp.einsum(
        "qhd,khd->hqk", grad_heads, value_all, preferred_element_type=jnp.float32
    )
    grad_scores = (weights * (grad_weights - row_delta[:, :, None]) * score_scale).astype(
        jnp.bfloat16
    )
    query_acc = jnp.einsum("hqk,khd->qhd", grad_scores, key_all, preferred_element_type=jnp.float32)
    stat_parts = split_three(jnp.concatenate([log_total, row_delta], axis=0))
    pair_width = 2 * flat_width
    stat_rows = -(-stat_parts.size // pair_width)
    stat_rows = -(-stat_rows // 16) * 16
    stat_block = jnp.pad(stat_parts.reshape(-1), (0, stat_rows * pair_width - stat_parts.size))
    packed_rows = jnp.concatenate(
        [
            jnp.concatenate([queries[0], grad_out], axis=1),
            stat_block.reshape(stat_rows, pair_width),
        ],
        axis=0,
    )
    query_grad = lax.all_gather(packed_rows, "tm", axis=0, tiled=False)
    query_pairs = query_grad[:, :frame_rows].reshape(total_frames, pair_width)
    stat_all = query_grad[:, frame_rows:].reshape(time_count, -1)[:, : stat_parts.size]
    stat_all = stat_all.reshape(time_count, stat_parts.shape[0], frame_rows)
    stat_all = join_three(jnp.transpose(stat_all, (1, 0, 2)).reshape(stat_parts.shape[0], -1))
    query_all = query_pairs[:, :flat_width].reshape(total_frames, HEADS, HDIM)
    grad_all = query_pairs[:, flat_width:].reshape(total_frames, HEADS, HDIM)
    log_total_all = stat_all[:HEADS]
    row_delta_all = stat_all[HEADS:]
    own_live = time_rank * frame_rows + jnp.arange(frame_rows, dtype=jnp.int32) < length
    scores_k = (
        jnp.einsum("qhd,khd->hqk", query_all, key_own, preferred_element_type=jnp.float32)
        * score_scale
    )
    scores_k = jnp.where(own_live[None, None, :], scores_k, NEG_FILL)
    weights_k = jnp.exp(scores_k - log_total_all[:, :, None])
    value_acc = jnp.einsum(
        "hqk,qhd->khd", weights_k.astype(jnp.bfloat16), grad_all, preferred_element_type=jnp.float32
    )
    grad_weights_k = jnp.einsum(
        "qhd,khd->hqk", grad_all, value_own, preferred_element_type=jnp.float32
    )
    grad_scores_k = (
        weights_k * (grad_weights_k - row_delta_all[:, :, None]) * score_scale
    ).astype(jnp.bfloat16)
    key_acc = jnp.einsum("hqk,qhd->khd", grad_scores_k, query_all, preferred_element_type=jnp.float32)
    grad_queries = query_acc.reshape(1, frame_rows, flat_width).astype(jnp.bfloat16)
    grad_keys = key_acc.reshape(1, frame_rows, flat_width).astype(jnp.bfloat16)
    grad_values = value_acc.reshape(1, frame_rows, flat_width).astype(jnp.bfloat16)
    half_width = (KW - 1) // 2
    frame_ids = time_rank * frame_rows + jnp.arange(frame_rows, dtype=jnp.int32)
    frame_live = (frame_ids < length).astype(jnp.float32)[:, None]
    glu_rows = glu_input[0]
    linear = glu_rows[:, :CH].astype(jnp.float32)
    gate_sig = jax.nn.sigmoid(glu_rows[:, CH:].astype(jnp.float32))
    activ = (linear * gate_sig * frame_live).astype(jnp.bfloat16)
    padded = extended(activ, (("tm", 0),), half_width)
    kernel_f = full_kernel.astype(jnp.float32)
    gain_f = full_gain.astype(jnp.float32)
    mixed = depthwise(padded, kernel_f, frame_rows)
    grad_conv, gain_term = norm_backward(mixed, gain_f, conv_upstream[0], frame_live)
    grad_pad = extended(grad_conv, (("tm", 0),), half_width)
    kernel_term = tap_products(grad_conv, padded, frame_rows, KW)
    grad_activ = back_depthwise(grad_pad, kernel_f, frame_rows) * frame_live
    first_half = grad_activ * gate_sig
    second_half = grad_activ * linear * gate_sig * (1.0 - gate_sig)
    grad_glu = jnp.concatenate([first_half, second_half], axis=-1).astype(jnp.bfloat16)[None]
    attended_flat = attended.reshape(frame_rows, flat_width)
    proj_term = lax.dot_general(
        upstream_rows,
        attended_flat,
        (((0,), (0,)), ((), ())),
        preferred_element_type=jnp.float32,
    )
    proj_total, kernel_total, gain_total = reduce_grads(proj_term, kernel_term, gain_term)
    grad_projection = proj_total.astype(jnp.bfloat16)
    return (
        grad_queries,
        grad_keys,
        grad_values,
        grad_projection,
        grad_glu,
        kernel_total,
        gain_total,
    )


def solution(mesh):
    in_specs = (
        P("dp", "tm", None),
        P("dp", "tm", None),
        P("dp", "tm", None),
        P("dp"),
        P("dp", None),
        P("dp", "tm", None),
        P("dp", "tm", None),
        P("dp", None),
        P("dp"),
        P("dp", "tm", None),
    )
    out_specs = (
        P("dp", "tm", None),
        P("dp", "tm", None),
        P("dp", "tm", None),
        P("dp", None),
        P("dp", "tm", None),
        P("dp", None),
        P("dp"),
    )
    return jax.shard_map(
        per_device, mesh=mesh, in_specs=in_specs, out_specs=out_specs, check_vma=False
    )
```

```python
import jax
import jax.numpy as jnp
from jax import lax
from jax.sharding import PartitionSpec as P

HEADS = 2
HDIM = 128
CH = 2048
KW = 31


NEG_FILL = -1e30
NORM_EPS = 1e-05


def from_behind(block, axis, distance):
    devices = range(lax.axis_size(axis))
    route = [((i - distance) % len(devices), i) for i in devices]
    return lax.ppermute(block, axis, route)


def extended(cells, sides, width):
    for axis, dim in sides:
        count = lax.axis_size(axis)
        ends = count - 1
        head = lax.slice_in_dim(cells, 0, width, axis=dim)
        tail = lax.slice_in_dim(cells, cells.shape[dim] - width, cells.shape[dim], axis=dim)
        cells = jnp.concatenate(
            [
                lax.ppermute(tail, axis, [(i, (i + 1) % count) for i in range(ends)]),
                cells,
                lax.ppermute(head, axis, [((i + 1) % count, i) for i in range(ends)]),
            ],
            axis=dim,
        )
    return cells


def depthwise(padded, kernel_f, frame_rows):
    mixed = jnp.zeros((frame_rows, kernel_f.shape[0]), jnp.float32)
    for tap in range(kernel_f.shape[1]):
        mixed = mixed + padded[tap : tap + frame_rows].astype(jnp.float32) * kernel_f[:, tap]
    return mixed


def back_depthwise(grad_pad, kernel_f, frame_rows):
    half_width = (kernel_f.shape[1] - 1) // 2
    result = jnp.zeros((frame_rows, kernel_f.shape[0]), jnp.float32)
    for tap in range(kernel_f.shape[1]):
        begin = 2 * half_width - tap
        result = (
            result + grad_pad[begin : begin + frame_rows].astype(jnp.float32) * kernel_f[:, tap]
        )
    return result


def tap_products(grad_low, padded, frame_rows, tap_count):
    grad_f = grad_low.astype(jnp.float32)
    return jnp.stack(
        [
            jnp.sum(grad_f * padded[tap : tap + frame_rows].astype(jnp.float32), axis=0)
            for tap in range(tap_count)
        ],
        axis=1,
    )


def norm_backward(mixed, gain_f, cotangent, frame_live):
    centre = mixed - jnp.mean(mixed, axis=-1, keepdims=True)
    inv_std = lax.rsqrt(jnp.mean(centre * centre, axis=-1, keepdims=True) + NORM_EPS)
    standard = centre * inv_std
    normed = standard * gain_f
    squash = jax.nn.sigmoid(normed)
    grad_normed = (
        cotangent.astype(jnp.float32) * frame_live * (squash + normed * squash * (1.0 - squash))
    )
    gain_term = jnp.sum(grad_normed * standard, axis=0)
    scaled = grad_normed * gain_f
    grad_conv = inv_std * (
        scaled
        - jnp.mean(scaled, axis=-1, keepdims=True)
        - standard * jnp.mean(scaled * standard, axis=-1, keepdims=True)
    )
    return (grad_conv.astype(jnp.bfloat16), gain_term)


def gather_params(projection, kernel, norm_gain):
    width = projection.shape[1]
    tail = jnp.concatenate([kernel.reshape(-1), norm_gain.reshape(-1)])
    tail_rows = -(-tail.shape[0] // width)
    tail = jnp.pad(tail, (0, tail_rows * width - tail.shape[0])).reshape(tail_rows, width)
    block = jnp.concatenate([projection, tail], axis=0)
    full = lax.all_gather(block, "dp", axis=0, tiled=False)
    count = full.shape[0]
    proj_rows = projection.shape[0]
    full_proj = full[:, :proj_rows].reshape(count * proj_rows, width)
    flat_tail = full[:, proj_rows:].reshape(count, tail_rows * width)
    kernel_size = kernel.shape[0] * kernel.shape[1]
    full_kernel = flat_tail[:, :kernel_size].reshape(count * kernel.shape[0], kernel.shape[1])
    full_gain = flat_tail[:, kernel_size : kernel_size + norm_gain.shape[0]].reshape(-1)
    return full_proj, full_kernel, full_gain


def reduce_grads(proj_term, kernel_term, gain_term):
    count = lax.axis_size("dp")
    width = proj_term.shape[1]
    proj_part = lax.psum_scatter(proj_term, "dp", scatter_dimension=0, tiled=True)
    proj_part, kernel_term, gain_term = lax.optimization_barrier((proj_part, kernel_term, gain_term))
    kernel_blocks = kernel_term.reshape(count, -1)
    gain_blocks = gain_term.reshape(count, -1)
    tail = jnp.concatenate([kernel_blocks, gain_blocks], axis=1)
    tail_cols = tail.shape[1]
    tail_rows = -(-tail_cols // width)
    tail = jnp.pad(tail, ((0, 0), (0, tail_rows * width - tail_cols))).reshape(-1, width)
    tail_part = lax.psum_scatter(tail, "dp", scatter_dimension=0, tiled=True)
    total = lax.psum(jnp.concatenate([proj_part, tail_part], axis=0), "tm")
    proj_rows = proj_part.shape[0]
    proj_total = total[:proj_rows]
    flat_tail = total[proj_rows:].reshape(-1)
    kernel_size = kernel_blocks.shape[1]
    kernel_total = flat_tail[:kernel_size].reshape(-1, kernel_term.shape[1])
    gain_total = flat_tail[kernel_size : kernel_size + gain_blocks.shape[1]]
    return proj_total, kernel_total, gain_total


def gather_tm(block):
    count = lax.axis_size("tm")
    parts = [block] + [
        lax.ppermute(block, "tm", [(i, (i + k) % count) for i in range(count)])
        for k in range(1, count)
    ]
    return jnp.stack(parts)


def split_three(values):
    high = lax.optimization_barrier(values.astype(jnp.bfloat16))
    rest = values - high.astype(jnp.float32)
    middle = lax.optimization_barrier(rest.astype(jnp.bfloat16))
    low = (rest - middle.astype(jnp.float32)).astype(jnp.bfloat16)
    return jnp.concatenate([high, middle, low], axis=0)


def join_three(parts):
    third = parts.shape[0] // 3
    wide = parts.astype(jnp.float32)
    return wide[:third] + wide[third : 2 * third] + wide[2 * third :]


def per_device(
    queries,
    key_input,
    value_input,
    lengths,
    projection,
    upstream,
    glu_input,
    kernel,
    norm_gain,
    conv_upstream,
):
    time_count = lax.axis_size("tm")
    time_rank = lax.axis_index("tm")
    frame_rows = queries.shape[1]
    flat_width = queries.shape[2]
    score_scale = HDIM ** (-0.5)
    length = lengths[0]
    full_proj, full_kernel, full_gain = gather_params(projection, kernel, norm_gain)
    query_heads = queries[0].reshape(frame_rows, HEADS, HDIM)
    key_own = key_input[0].reshape(frame_rows, HEADS, HDIM)
    value_own = value_input[0].reshape(frame_rows, HEADS, HDIM)
    key_value = gather_tm(jnp.concatenate([key_input[0], value_input[0]], axis=1))
    key_source = (time_rank - jnp.arange(time_count, dtype=jnp.int32)) % time_count
    key_frames = key_source[:, None] * frame_rows + jnp.arange(frame_rows, dtype=jnp.int32)
    key_value = key_value.reshape(-1, key_value.shape[-1])
    total_frames = key_value.shape[0]
    key_all = key_value[:, :flat_width].reshape(total_frames, HEADS, HDIM)
    value_all = key_value[:, flat_width:].reshape(total_frames, HEADS, HDIM)
    key_live = key_frames.reshape(-1) < length
    scores = (
        jnp.einsum("qhd,khd->hqk", query_heads, key_all, preferred_element_type=jnp.float32)
        * score_scale
    )
    scores = jnp.where(key_live[None, None, :], scores, NEG_FILL)
    row_top = jnp.max(scores, axis=-1)
    log_total = row_top + jnp.log(jnp.sum(jnp.exp(scores - row_top[:, :, None]), axis=-1))
    weights = jnp.exp(scores - log_total[:, :, None])
    weights_high = lax.optimization_barrier(weights.astype(jnp.bfloat16))
    weights_rest = (weights - weights_high.astype(jnp.float32)).astype(jnp.bfloat16)
    attended = (
        jnp.einsum("hqk,khd->qhd", weights_high, value_all, preferred_element_type=jnp.float32)
        + jnp.einsum("hqk,khd->qhd", weights_rest, value_all, preferred_element_type=jnp.float32)
    ).astype(jnp.bfloat16)
    upstream_rows = upstream[0]
    grad_out = jnp.dot(upstream_rows, full_proj, preferred_element_type=jnp.float32).astype(
        jnp.bfloat16
    )
    grad_heads = grad_out.reshape(frame_rows, HEADS, HDIM)
    row_delta = jnp.einsum("qhd,qhd->hq", grad_heads, attended, preferred_element_type=jnp.float32)
    grad_weights = jnp.einsum(
        "qhd,khd->hqk", grad_heads, value_all, preferred_element_type=jnp.float32
    )
    grad_scores = (weights * (grad_weights - row_delta[:, :, None]) * score_scale).astype(
        jnp.bfloat16
    )
    query_acc = jnp.einsum("hqk,khd->qhd", grad_scores, key_all, preferred_element_type=jnp.float32)
    stat_parts = split_three(jnp.concatenate([log_total, row_delta], axis=0))
    pair_width = 2 * flat_width
    stat_rows = -(-stat_parts.size // pair_width)
    stat_rows = -(-stat_rows // 16) * 16
    stat_block = jnp.pad(stat_parts.reshape(-1), (0, stat_rows * pair_width - stat_parts.size))
    packed_rows = jnp.concatenate(
        [
            jnp.concatenate([queries[0], grad_out], axis=1),
            stat_block.reshape(stat_rows, pair_width),
        ],
        axis=0,
    )
    query_grad = gather_tm(packed_rows)
    query_pairs = query_grad[:, :frame_rows].reshape(total_frames, pair_width)
    stat_all = query_grad[:, frame_rows:].reshape(time_count, -1)[:, : stat_parts.size]
    stat_all = stat_all.reshape(time_count, stat_parts.shape[0], frame_rows)
    stat_all = join_three(jnp.transpose(stat_all, (1, 0, 2)).reshape(stat_parts.shape[0], -1))
    query_all = query_pairs[:, :flat_width].reshape(total_frames, HEADS, HDIM)
    grad_all = query_pairs[:, flat_width:].reshape(total_frames, HEADS, HDIM)
    log_total_all = stat_all[:HEADS]
    row_delta_all = stat_all[HEADS:]
    own_live = time_rank * frame_rows + jnp.arange(frame_rows, dtype=jnp.int32) < length
    scores_k = (
        jnp.einsum("qhd,khd->hqk", query_all, key_own, preferred_element_type=jnp.float32)
        * score_scale
    )
    scores_k = jnp.where(own_live[None, None, :], scores_k, NEG_FILL)
    weights_k = jnp.exp(scores_k - log_total_all[:, :, None])
    value_acc = jnp.einsum(
        "hqk,qhd->khd", weights_k.astype(jnp.bfloat16), grad_all, preferred_element_type=jnp.float32
    )
    grad_weights_k = jnp.einsum(
        "qhd,khd->hqk", grad_all, value_own, preferred_element_type=jnp.float32
    )
    grad_scores_k = (
        weights_k * (grad_weights_k - row_delta_all[:, :, None]) * score_scale
    ).astype(jnp.bfloat16)
    key_acc = jnp.einsum("hqk,qhd->khd", grad_scores_k, query_all, preferred_element_type=jnp.float32)
    grad_queries = query_acc.reshape(1, frame_rows, flat_width).astype(jnp.bfloat16)
    grad_keys = key_acc.reshape(1, frame_rows, flat_width).astype(jnp.bfloat16)
    grad_values = value_acc.reshape(1, frame_rows, flat_width).astype(jnp.bfloat16)
    half_width = (KW - 1) // 2
    frame_ids = time_rank * frame_rows + jnp.arange(frame_rows, dtype=jnp.int32)
    frame_live = (frame_ids < length).astype(jnp.float32)[:, None]
    glu_rows = glu_input[0]
    linear = glu_rows[:, :CH].astype(jnp.float32)
    gate_sig = jax.nn.sigmoid(glu_rows[:, CH:].astype(jnp.float32))
    activ = (linear * gate_sig * frame_live).astype(jnp.bfloat16)
    padded = extended(activ, (("tm", 0),), half_width)
    kernel_f = full_kernel.astype(jnp.float32)
    gain_f = full_gain.astype(jnp.float32)
    mixed = depthwise(padded, kernel_f, frame_rows)
    attended_flat = attended.reshape(frame_rows, flat_width)
    proj_term = lax.dot_general(
        upstream_rows,
        attended_flat,
        (((0,), (0,)), ((), ())),
        preferred_element_type=jnp.float32,
    )
    proj_term, mixed = lax.optimization_barrier((proj_term, mixed))
    grad_conv, gain_term = norm_backward(mixed, gain_f, conv_upstream[0], frame_live)
    grad_pad = extended(grad_conv, (("tm", 0),), half_width)
    kernel_term = tap_products(grad_conv, padded, frame_rows, KW)
    grad_activ = back_depthwise(grad_pad, kernel_f, frame_rows) * frame_live
    first_half = grad_activ * gate_sig
    second_half = grad_activ * linear * gate_sig * (1.0 - gate_sig)
    grad_glu = jnp.concatenate([first_half, second_half], axis=-1).astype(jnp.bfloat16)[None]
    proj_total, kernel_total, gain_total = reduce_grads(proj_term, kernel_term, gain_term)
    grad_projection = proj_total.astype(jnp.bfloat16)
    return (
        grad_queries,
        grad_keys,
        grad_values,
        grad_projection,
        grad_glu,
        kernel_total,
        gain_total,
    )


def solution(mesh):
    in_specs = (
        P("dp", "tm", None),
        P("dp", "tm", None),
        P("dp", "tm", None),
        P("dp"),
        P("dp", None),
        P("dp", "tm", None),
        P("dp", "tm", None),
        P("dp", None),
        P("dp"),
        P("dp", "tm", None),
    )
    out_specs = (
        P("dp", "tm", None),
        P("dp", "tm", None),
        P("dp", "tm", None),
        P("dp", None),
        P("dp", "tm", None),
        P("dp", None),
        P("dp"),
    )
    return jax.shard_map(
        per_device, mesh=mesh, in_specs=in_specs, out_specs=out_specs, check_vma=False
    )
```

```python
import jax
import jax.numpy as jnp
from jax import lax
from jax.sharding import PartitionSpec as P

HEADS = 2
HDIM = 128
CH = 2048
KW = 31


NEG_FILL = -1e30
NORM_EPS = 1e-05


def from_behind(block, axis, distance):
    devices = range(lax.axis_size(axis))
    route = [((i - distance) % len(devices), i) for i in devices]
    return lax.ppermute(block, axis, route)


def extended(cells, sides, width):
    for axis, dim in sides:
        count = lax.axis_size(axis)
        ends = count - 1
        head = lax.slice_in_dim(cells, 0, width, axis=dim)
        tail = lax.slice_in_dim(cells, cells.shape[dim] - width, cells.shape[dim], axis=dim)
        cells = jnp.concatenate(
            [
                lax.ppermute(tail, axis, [(i, (i + 1) % count) for i in range(ends)]),
                cells,
                lax.ppermute(head, axis, [((i + 1) % count, i) for i in range(ends)]),
            ],
            axis=dim,
        )
    return cells


def depthwise(padded, kernel_f, frame_rows):
    mixed = jnp.zeros((frame_rows, kernel_f.shape[0]), jnp.float32)
    for tap in range(kernel_f.shape[1]):
        mixed = mixed + padded[tap : tap + frame_rows].astype(jnp.float32) * kernel_f[:, tap]
    return mixed


def back_depthwise(grad_pad, kernel_f, frame_rows):
    half_width = (kernel_f.shape[1] - 1) // 2
    result = jnp.zeros((frame_rows, kernel_f.shape[0]), jnp.float32)
    for tap in range(kernel_f.shape[1]):
        begin = 2 * half_width - tap
        result = (
            result + grad_pad[begin : begin + frame_rows].astype(jnp.float32) * kernel_f[:, tap]
        )
    return result


def tap_products(grad_low, padded, frame_rows, tap_count):
    grad_f = grad_low.astype(jnp.float32)
    return jnp.stack(
        [
            jnp.sum(grad_f * padded[tap : tap + frame_rows].astype(jnp.float32), axis=0)
            for tap in range(tap_count)
        ],
        axis=1,
    )


def norm_backward(mixed, gain_f, cotangent, frame_live):
    centre = mixed - jnp.mean(mixed, axis=-1, keepdims=True)
    inv_std = lax.rsqrt(jnp.mean(centre * centre, axis=-1, keepdims=True) + NORM_EPS)
    standard = centre * inv_std
    normed = standard * gain_f
    squash = jax.nn.sigmoid(normed)
    grad_normed = (
        cotangent.astype(jnp.float32) * frame_live * (squash + normed * squash * (1.0 - squash))
    )
    gain_term = jnp.sum(grad_normed * standard, axis=0)
    scaled = grad_normed * gain_f
    grad_conv = inv_std * (
        scaled
        - jnp.mean(scaled, axis=-1, keepdims=True)
        - standard * jnp.mean(scaled * standard, axis=-1, keepdims=True)
    )
    return (grad_conv.astype(jnp.bfloat16), gain_term)


def gather_params(projection, kernel, norm_gain):
    width = projection.shape[1]
    tail = jnp.concatenate([kernel.reshape(-1), norm_gain.reshape(-1)])
    tail_rows = -(-tail.shape[0] // width)
    tail = jnp.pad(tail, (0, tail_rows * width - tail.shape[0])).reshape(tail_rows, width)
    block = jnp.concatenate([projection, tail], axis=0)
    full = lax.all_gather(block, "dp", axis=0, tiled=False)
    count = full.shape[0]
    proj_rows = projection.shape[0]
    full_proj = full[:, :proj_rows].reshape(count * proj_rows, width)
    flat_tail = full[:, proj_rows:].reshape(count, tail_rows * width)
    kernel_size = kernel.shape[0] * kernel.shape[1]
    full_kernel = flat_tail[:, :kernel_size].reshape(count * kernel.shape[0], kernel.shape[1])
    full_gain = flat_tail[:, kernel_size : kernel_size + norm_gain.shape[0]].reshape(-1)
    return full_proj, full_kernel, full_gain


def spread_sum(blocks):
    count = lax.axis_size("tm")
    rank = lax.axis_index("tm")
    owners, rows, width = blocks.shape
    chunks = jnp.transpose(blocks.reshape(owners, count, rows // count, width), (1, 0, 2, 3))
    total = lax.dynamic_index_in_dim(chunks, rank, 0, keepdims=False)
    for k in range(1, count):
        outgoing = lax.dynamic_index_in_dim(chunks, (rank + k) % count, 0, keepdims=False)
        total = total + lax.ppermute(outgoing, "tm", [(i, (i + k) % count) for i in range(count)])
    part = lax.psum_scatter(total.reshape(-1, width), "dp", scatter_dimension=0, tiled=True)
    parts = gather_tm(part)
    order = (rank - jnp.arange(count, dtype=jnp.int32)) % count
    return jnp.take(parts, order, axis=0).reshape(rows, width)


def reduce_grads(proj_term, kernel_term, gain_term):
    count = lax.axis_size("dp")
    width = proj_term.shape[1]
    proj_total = spread_sum(proj_term.reshape(count, -1, width))
    kernel_blocks = kernel_term.reshape(count, -1)
    gain_blocks = gain_term.reshape(count, -1)
    tail = jnp.concatenate([kernel_blocks, gain_blocks], axis=1)
    tail_cols = tail.shape[1]
    tail_rows = -(-tail_cols // width)
    tail = jnp.pad(tail, ((0, 0), (0, tail_rows * width - tail_cols))).reshape(
        count, tail_rows, width
    )
    flat_tail = spread_sum(tail).reshape(-1)
    kernel_size = kernel_blocks.shape[1]
    kernel_total = flat_tail[:kernel_size].reshape(-1, kernel_term.shape[1])
    gain_total = flat_tail[kernel_size : kernel_size + gain_blocks.shape[1]]
    return proj_total, kernel_total, gain_total


def gather_tm(block):
    count = lax.axis_size("tm")
    parts = [block] + [
        lax.ppermute(block, "tm", [(i, (i + k) % count) for i in range(count)])
        for k in range(1, count)
    ]
    return jnp.stack(parts)


def split_three(values):
    high = lax.optimization_barrier(values.astype(jnp.bfloat16))
    rest = values - high.astype(jnp.float32)
    middle = lax.optimization_barrier(rest.astype(jnp.bfloat16))
    low = (rest - middle.astype(jnp.float32)).astype(jnp.bfloat16)
    return jnp.concatenate([high, middle, low], axis=0)


def join_three(parts):
    third = parts.shape[0] // 3
    wide = parts.astype(jnp.float32)
    return wide[:third] + wide[third : 2 * third] + wide[2 * third :]


def per_device(
    queries,
    key_input,
    value_input,
    lengths,
    projection,
    upstream,
    glu_input,
    kernel,
    norm_gain,
    conv_upstream,
):
    time_count = lax.axis_size("tm")
    time_rank = lax.axis_index("tm")
    frame_rows = queries.shape[1]
    flat_width = queries.shape[2]
    score_scale = HDIM ** (-0.5)
    length = lengths[0]
    full_proj, full_kernel, full_gain = gather_params(projection, kernel, norm_gain)
    query_heads = queries[0].reshape(frame_rows, HEADS, HDIM)
    key_own = key_input[0].reshape(frame_rows, HEADS, HDIM)
    value_own = value_input[0].reshape(frame_rows, HEADS, HDIM)
    key_value = gather_tm(jnp.concatenate([key_input[0], value_input[0]], axis=1))
    key_source = (time_rank - jnp.arange(time_count, dtype=jnp.int32)) % time_count
    key_frames = key_source[:, None] * frame_rows + jnp.arange(frame_rows, dtype=jnp.int32)
    key_value = key_value.reshape(-1, key_value.shape[-1])
    total_frames = key_value.shape[0]
    key_all = key_value[:, :flat_width].reshape(total_frames, HEADS, HDIM)
    value_all = key_value[:, flat_width:].reshape(total_frames, HEADS, HDIM)
    key_live = key_frames.reshape(-1) < length
    scores = (
        jnp.einsum("qhd,khd->hqk", query_heads, key_all, preferred_element_type=jnp.float32)
        * score_scale
    )
    scores = jnp.where(key_live[None, None, :], scores, NEG_FILL)
    row_top = jnp.max(scores, axis=-1)
    log_total = row_top + jnp.log(jnp.sum(jnp.exp(scores - row_top[:, :, None]), axis=-1))
    weights = jnp.exp(scores - log_total[:, :, None])
    weights_high = lax.optimization_barrier(weights.astype(jnp.bfloat16))
    weights_rest = (weights - weights_high.astype(jnp.float32)).astype(jnp.bfloat16)
    attended = (
        jnp.einsum("hqk,khd->qhd", weights_high, value_all, preferred_element_type=jnp.float32)
        + jnp.einsum("hqk,khd->qhd", weights_rest, value_all, preferred_element_type=jnp.float32)
    ).astype(jnp.bfloat16)
    upstream_rows = upstream[0]
    grad_out = jnp.dot(upstream_rows, full_proj, preferred_element_type=jnp.float32).astype(
        jnp.bfloat16
    )
    grad_heads = grad_out.reshape(frame_rows, HEADS, HDIM)
    row_delta = jnp.einsum("qhd,qhd->hq", grad_heads, attended, preferred_element_type=jnp.float32)
    grad_weights = jnp.einsum(
        "qhd,khd->hqk", grad_heads, value_all, preferred_element_type=jnp.float32
    )
    grad_scores = (weights * (grad_weights - row_delta[:, :, None]) * score_scale).astype(
        jnp.bfloat16
    )
    query_acc = jnp.einsum("hqk,khd->qhd", grad_scores, key_all, preferred_element_type=jnp.float32)
    stat_parts = split_three(jnp.concatenate([log_total, row_delta], axis=0))
    pair_width = 2 * flat_width
    stat_rows = -(-stat_parts.size // pair_width)
    stat_rows = -(-stat_rows // 16) * 16
    stat_block = jnp.pad(stat_parts.reshape(-1), (0, stat_rows * pair_width - stat_parts.size))
    packed_rows = jnp.concatenate(
        [
            jnp.concatenate([queries[0], grad_out], axis=1),
            stat_block.reshape(stat_rows, pair_width),
        ],
        axis=0,
    )
    query_grad = gather_tm(packed_rows)
    query_pairs = query_grad[:, :frame_rows].reshape(total_frames, pair_width)
    stat_all = query_grad[:, frame_rows:].reshape(time_count, -1)[:, : stat_parts.size]
    stat_all = stat_all.reshape(time_count, stat_parts.shape[0], frame_rows)
    stat_all = join_three(jnp.transpose(stat_all, (1, 0, 2)).reshape(stat_parts.shape[0], -1))
    query_all = query_pairs[:, :flat_width].reshape(total_frames, HEADS, HDIM)
    grad_all = query_pairs[:, flat_width:].reshape(total_frames, HEADS, HDIM)
    log_total_all = stat_all[:HEADS]
    row_delta_all = stat_all[HEADS:]
    own_live = time_rank * frame_rows + jnp.arange(frame_rows, dtype=jnp.int32) < length
    scores_k = (
        jnp.einsum("qhd,khd->hqk", query_all, key_own, preferred_element_type=jnp.float32)
        * score_scale
    )
    scores_k = jnp.where(own_live[None, None, :], scores_k, NEG_FILL)
    weights_k = jnp.exp(scores_k - log_total_all[:, :, None])
    value_acc = jnp.einsum(
        "hqk,qhd->khd", weights_k.astype(jnp.bfloat16), grad_all, preferred_element_type=jnp.float32
    )
    grad_weights_k = jnp.einsum(
        "qhd,khd->hqk", grad_all, value_own, preferred_element_type=jnp.float32
    )
    grad_scores_k = (
        weights_k * (grad_weights_k - row_delta_all[:, :, None]) * score_scale
    ).astype(jnp.bfloat16)
    key_acc = jnp.einsum("hqk,qhd->khd", grad_scores_k, query_all, preferred_element_type=jnp.float32)
    grad_queries = query_acc.reshape(1, frame_rows, flat_width).astype(jnp.bfloat16)
    grad_keys = key_acc.reshape(1, frame_rows, flat_width).astype(jnp.bfloat16)
    grad_values = value_acc.reshape(1, frame_rows, flat_width).astype(jnp.bfloat16)
    half_width = (KW - 1) // 2
    frame_ids = time_rank * frame_rows + jnp.arange(frame_rows, dtype=jnp.int32)
    frame_live = (frame_ids < length).astype(jnp.float32)[:, None]
    glu_rows = glu_input[0]
    linear = glu_rows[:, :CH].astype(jnp.float32)
    gate_sig = jax.nn.sigmoid(glu_rows[:, CH:].astype(jnp.float32))
    activ = (linear * gate_sig * frame_live).astype(jnp.bfloat16)
    padded = extended(activ, (("tm", 0),), half_width)
    kernel_f = full_kernel.astype(jnp.float32)
    gain_f = full_gain.astype(jnp.float32)
    mixed = depthwise(padded, kernel_f, frame_rows)
    attended_flat = attended.reshape(frame_rows, flat_width)
    proj_term = lax.dot_general(
        upstream_rows,
        attended_flat,
        (((0,), (0,)), ((), ())),
        preferred_element_type=jnp.float32,
    )
    proj_term, mixed = lax.optimization_barrier((proj_term, mixed))
    grad_conv, gain_term = norm_backward(mixed, gain_f, conv_upstream[0], frame_live)
    grad_pad = extended(grad_conv, (("tm", 0),), half_width)
    kernel_term = tap_products(grad_conv, padded, frame_rows, KW)
    grad_activ = back_depthwise(grad_pad, kernel_f, frame_rows) * frame_live
    first_half = grad_activ * gate_sig
    second_half = grad_activ * linear * gate_sig * (1.0 - gate_sig)
    grad_glu = jnp.concatenate([first_half, second_half], axis=-1).astype(jnp.bfloat16)[None]
    proj_total, kernel_total, gain_total = reduce_grads(proj_term, kernel_term, gain_term)
    grad_projection = proj_total.astype(jnp.bfloat16)
    return (
        grad_queries,
        grad_keys,
        grad_values,
        grad_projection,
        grad_glu,
        kernel_total,
        gain_total,
    )


def solution(mesh):
    in_specs = (
        P("dp", "tm", None),
        P("dp", "tm", None),
        P("dp", "tm", None),
        P("dp"),
        P("dp", None),
        P("dp", "tm", None),
        P("dp", "tm", None),
        P("dp", None),
        P("dp"),
        P("dp", "tm", None),
    )
    out_specs = (
        P("dp", "tm", None),
        P("dp", "tm", None),
        P("dp", "tm", None),
        P("dp", None),
        P("dp", "tm", None),
        P("dp", None),
        P("dp"),
    )
    return jax.shard_map(
        per_device, mesh=mesh, in_specs=in_specs, out_specs=out_specs, check_vma=False
    )
```

```python
import jax
import jax.numpy as jnp
from jax import lax
from jax.sharding import PartitionSpec as P

HEADS = 2
HDIM = 128
CH = 2048
KW = 31


NEG_FILL = -1e30
NORM_EPS = 1e-05


def from_behind(block, axis, distance):
    devices = range(lax.axis_size(axis))
    route = [((i - distance) % len(devices), i) for i in devices]
    return lax.ppermute(block, axis, route)


def extended(cells, sides, width):
    for axis, dim in sides:
        count = lax.axis_size(axis)
        ends = count - 1
        head = lax.slice_in_dim(cells, 0, width, axis=dim)
        tail = lax.slice_in_dim(cells, cells.shape[dim] - width, cells.shape[dim], axis=dim)
        cells = jnp.concatenate(
            [
                lax.ppermute(tail, axis, [(i, (i + 1) % count) for i in range(ends)]),
                cells,
                lax.ppermute(head, axis, [((i + 1) % count, i) for i in range(ends)]),
            ],
            axis=dim,
        )
    return cells


def depthwise(padded, kernel_f, frame_rows):
    mixed = jnp.zeros((frame_rows, kernel_f.shape[0]), jnp.float32)
    for tap in range(kernel_f.shape[1]):
        mixed = mixed + padded[tap : tap + frame_rows].astype(jnp.float32) * kernel_f[:, tap]
    return mixed


def back_depthwise(grad_pad, kernel_f, frame_rows):
    half_width = (kernel_f.shape[1] - 1) // 2
    result = jnp.zeros((frame_rows, kernel_f.shape[0]), jnp.float32)
    for tap in range(kernel_f.shape[1]):
        begin = 2 * half_width - tap
        result = (
            result + grad_pad[begin : begin + frame_rows].astype(jnp.float32) * kernel_f[:, tap]
        )
    return result


def tap_products(grad_low, padded, frame_rows, tap_count):
    grad_f = grad_low.astype(jnp.float32)
    return jnp.stack(
        [
            jnp.sum(grad_f * padded[tap : tap + frame_rows].astype(jnp.float32), axis=0)
            for tap in range(tap_count)
        ],
        axis=1,
    )


def norm_backward(mixed, gain_f, cotangent, frame_live):
    centre = mixed - jnp.mean(mixed, axis=-1, keepdims=True)
    inv_std = lax.rsqrt(jnp.mean(centre * centre, axis=-1, keepdims=True) + NORM_EPS)
    standard = centre * inv_std
    normed = standard * gain_f
    squash = jax.nn.sigmoid(normed)
    grad_normed = (
        cotangent.astype(jnp.float32) * frame_live * (squash + normed * squash * (1.0 - squash))
    )
    gain_term = jnp.sum(grad_normed * standard, axis=0)
    scaled = grad_normed * gain_f
    grad_conv = inv_std * (
        scaled
        - jnp.mean(scaled, axis=-1, keepdims=True)
        - standard * jnp.mean(scaled * standard, axis=-1, keepdims=True)
    )
    return (grad_conv.astype(jnp.bfloat16), gain_term)


def gather_params(projection, kernel, norm_gain):
    width = projection.shape[1]
    tail = jnp.concatenate([kernel.reshape(-1), norm_gain.reshape(-1)])
    tail_rows = -(-tail.shape[0] // width)
    tail = jnp.pad(tail, (0, tail_rows * width - tail.shape[0])).reshape(tail_rows, width)
    block = jnp.concatenate([projection, tail], axis=0)
    full = lax.all_gather(block, "dp", axis=0, tiled=False)
    count = full.shape[0]
    proj_rows = projection.shape[0]
    full_proj = full[:, :proj_rows].reshape(count * proj_rows, width)
    flat_tail = full[:, proj_rows:].reshape(count, tail_rows * width)
    kernel_size = kernel.shape[0] * kernel.shape[1]
    full_kernel = flat_tail[:, :kernel_size].reshape(count * kernel.shape[0], kernel.shape[1])
    full_gain = flat_tail[:, kernel_size : kernel_size + norm_gain.shape[0]].reshape(-1)
    return full_proj, full_kernel, full_gain


def spread_sum(blocks):
    count = lax.axis_size("tm")
    rank = lax.axis_index("tm")
    owners, rows, width = blocks.shape
    chunks = jnp.transpose(blocks.reshape(owners, count, rows // count, width), (1, 0, 2, 3))
    total = lax.dynamic_index_in_dim(chunks, rank, 0, keepdims=False)
    for k in range(1, count):
        outgoing = lax.dynamic_index_in_dim(chunks, (rank + k) % count, 0, keepdims=False)
        total = total + lax.ppermute(outgoing, "tm", [(i, (i + k) % count) for i in range(count)])
    part = lax.psum_scatter(total.reshape(-1, width), "dp", scatter_dimension=0, tiled=True)
    parts = gather_tm(part)
    order = (rank - jnp.arange(count, dtype=jnp.int32)) % count
    return jnp.take(parts, order, axis=0).reshape(rows, width)


def reduce_grads(proj_term, kernel_term, gain_term):
    count = lax.axis_size("dp")
    width = proj_term.shape[1]
    proj_total = spread_sum(proj_term.reshape(count, -1, width))
    kernel_blocks = kernel_term.reshape(count, -1)
    gain_blocks = gain_term.reshape(count, -1)
    tail = jnp.concatenate([kernel_blocks, gain_blocks], axis=1)
    tail_cols = tail.shape[1]
    tail_rows = -(-tail_cols // width)
    tail = jnp.pad(tail, ((0, 0), (0, tail_rows * width - tail_cols))).reshape(
        count, tail_rows, width
    )
    tail_part = lax.psum_scatter(tail.reshape(-1, width), "dp", scatter_dimension=0, tiled=True)
    flat_tail = lax.psum(tail_part, "tm").reshape(-1)
    kernel_size = kernel_blocks.shape[1]
    kernel_total = flat_tail[:kernel_size].reshape(-1, kernel_term.shape[1])
    gain_total = flat_tail[kernel_size : kernel_size + gain_blocks.shape[1]]
    return proj_total, kernel_total, gain_total


def gather_tm(block):
    count = lax.axis_size("tm")
    parts = [block] + [
        lax.ppermute(block, "tm", [(i, (i + k) % count) for i in range(count)])
        for k in range(1, count)
    ]
    return jnp.stack(parts)


def split_three(values):
    high = lax.optimization_barrier(values.astype(jnp.bfloat16))
    rest = values - high.astype(jnp.float32)
    middle = lax.optimization_barrier(rest.astype(jnp.bfloat16))
    low = (rest - middle.astype(jnp.float32)).astype(jnp.bfloat16)
    return jnp.concatenate([high, middle, low], axis=0)


def join_three(parts):
    third = parts.shape[0] // 3
    wide = parts.astype(jnp.float32)
    return wide[:third] + wide[third : 2 * third] + wide[2 * third :]


def per_device(
    queries,
    key_input,
    value_input,
    lengths,
    projection,
    upstream,
    glu_input,
    kernel,
    norm_gain,
    conv_upstream,
):
    time_count = lax.axis_size("tm")
    time_rank = lax.axis_index("tm")
    frame_rows = queries.shape[1]
    flat_width = queries.shape[2]
    score_scale = HDIM ** (-0.5)
    length = lengths[0]
    full_proj, full_kernel, full_gain = gather_params(projection, kernel, norm_gain)
    query_heads = queries[0].reshape(frame_rows, HEADS, HDIM)
    key_own = key_input[0].reshape(frame_rows, HEADS, HDIM)
    value_own = value_input[0].reshape(frame_rows, HEADS, HDIM)
    key_value = gather_tm(jnp.concatenate([key_input[0], value_input[0]], axis=1))
    key_source = (time_rank - jnp.arange(time_count, dtype=jnp.int32)) % time_count
    key_frames = key_source[:, None] * frame_rows + jnp.arange(frame_rows, dtype=jnp.int32)
    key_value = key_value.reshape(-1, key_value.shape[-1])
    total_frames = key_value.shape[0]
    key_all = key_value[:, :flat_width].reshape(total_frames, HEADS, HDIM)
    value_all = key_value[:, flat_width:].reshape(total_frames, HEADS, HDIM)
    key_live = key_frames.reshape(-1) < length
    scores = (
        jnp.einsum("qhd,khd->hqk", query_heads, key_all, preferred_element_type=jnp.float32)
        * score_scale
    )
    scores = jnp.where(key_live[None, None, :], scores, NEG_FILL)
    row_top = jnp.max(scores, axis=-1)
    log_total = row_top + jnp.log(jnp.sum(jnp.exp(scores - row_top[:, :, None]), axis=-1))
    weights = jnp.exp(scores - log_total[:, :, None])
    weights_high = lax.optimization_barrier(weights.astype(jnp.bfloat16))
    weights_rest = (weights - weights_high.astype(jnp.float32)).astype(jnp.bfloat16)
    attended = (
        jnp.einsum("hqk,khd->qhd", weights_high, value_all, preferred_element_type=jnp.float32)
        + jnp.einsum("hqk,khd->qhd", weights_rest, value_all, preferred_element_type=jnp.float32)
    ).astype(jnp.bfloat16)
    upstream_rows = upstream[0]
    grad_out = jnp.dot(upstream_rows, full_proj, preferred_element_type=jnp.float32).astype(
        jnp.bfloat16
    )
    grad_heads = grad_out.reshape(frame_rows, HEADS, HDIM)
    row_delta = jnp.einsum("qhd,qhd->hq", grad_heads, attended, preferred_element_type=jnp.float32)
    grad_weights = jnp.einsum(
        "qhd,khd->hqk", grad_heads, value_all, preferred_element_type=jnp.float32
    )
    grad_scores = (weights * (grad_weights - row_delta[:, :, None]) * score_scale).astype(
        jnp.bfloat16
    )
    query_acc = jnp.einsum("hqk,khd->qhd", grad_scores, key_all, preferred_element_type=jnp.float32)
    stat_parts = split_three(jnp.concatenate([log_total, row_delta], axis=0))
    pair_width = 2 * flat_width
    stat_rows = -(-stat_parts.size // pair_width)
    stat_rows = -(-stat_rows // 16) * 16
    stat_block = jnp.pad(stat_parts.reshape(-1), (0, stat_rows * pair_width - stat_parts.size))
    packed_rows = jnp.concatenate(
        [
            jnp.concatenate([queries[0], grad_out], axis=1),
            stat_block.reshape(stat_rows, pair_width),
        ],
        axis=0,
    )
    query_grad = gather_tm(packed_rows)
    query_pairs = query_grad[:, :frame_rows].reshape(total_frames, pair_width)
    stat_all = query_grad[:, frame_rows:].reshape(time_count, -1)[:, : stat_parts.size]
    stat_all = stat_all.reshape(time_count, stat_parts.shape[0], frame_rows)
    stat_all = join_three(jnp.transpose(stat_all, (1, 0, 2)).reshape(stat_parts.shape[0], -1))
    query_all = query_pairs[:, :flat_width].reshape(total_frames, HEADS, HDIM)
    grad_all = query_pairs[:, flat_width:].reshape(total_frames, HEADS, HDIM)
    log_total_all = stat_all[:HEADS]
    row_delta_all = stat_all[HEADS:]
    own_live = time_rank * frame_rows + jnp.arange(frame_rows, dtype=jnp.int32) < length
    scores_k = (
        jnp.einsum("qhd,khd->hqk", query_all, key_own, preferred_element_type=jnp.float32)
        * score_scale
    )
    scores_k = jnp.where(own_live[None, None, :], scores_k, NEG_FILL)
    weights_k = jnp.exp(scores_k - log_total_all[:, :, None])
    value_acc = jnp.einsum(
        "hqk,qhd->khd", weights_k.astype(jnp.bfloat16), grad_all, preferred_element_type=jnp.float32
    )
    grad_weights_k = jnp.einsum(
        "qhd,khd->hqk", grad_all, value_own, preferred_element_type=jnp.float32
    )
    grad_scores_k = (
        weights_k * (grad_weights_k - row_delta_all[:, :, None]) * score_scale
    ).astype(jnp.bfloat16)
    key_acc = jnp.einsum("hqk,qhd->khd", grad_scores_k, query_all, preferred_element_type=jnp.float32)
    grad_queries = query_acc.reshape(1, frame_rows, flat_width).astype(jnp.bfloat16)
    grad_keys = key_acc.reshape(1, frame_rows, flat_width).astype(jnp.bfloat16)
    grad_values = value_acc.reshape(1, frame_rows, flat_width).astype(jnp.bfloat16)
    half_width = (KW - 1) // 2
    frame_ids = time_rank * frame_rows + jnp.arange(frame_rows, dtype=jnp.int32)
    frame_live = (frame_ids < length).astype(jnp.float32)[:, None]
    glu_rows = glu_input[0]
    linear = glu_rows[:, :CH].astype(jnp.float32)
    gate_sig = jax.nn.sigmoid(glu_rows[:, CH:].astype(jnp.float32))
    activ = (linear * gate_sig * frame_live).astype(jnp.bfloat16)
    padded = extended(activ, (("tm", 0),), half_width)
    kernel_f = full_kernel.astype(jnp.float32)
    gain_f = full_gain.astype(jnp.float32)
    mixed = depthwise(padded, kernel_f, frame_rows)
    attended_flat = attended.reshape(frame_rows, flat_width)
    proj_term = lax.dot_general(
        upstream_rows,
        attended_flat,
        (((0,), (0,)), ((), ())),
        preferred_element_type=jnp.float32,
    )
    proj_term, mixed = lax.optimization_barrier((proj_term, mixed))
    grad_conv, gain_term = norm_backward(mixed, gain_f, conv_upstream[0], frame_live)
    grad_pad = extended(grad_conv, (("tm", 0),), half_width)
    kernel_term = tap_products(grad_conv, padded, frame_rows, KW)
    grad_activ = back_depthwise(grad_pad, kernel_f, frame_rows) * frame_live
    first_half = grad_activ * gate_sig
    second_half = grad_activ * linear * gate_sig * (1.0 - gate_sig)
    grad_glu = jnp.concatenate([first_half, second_half], axis=-1).astype(jnp.bfloat16)[None]
    proj_total, kernel_total, gain_total = reduce_grads(proj_term, kernel_term, gain_term)
    grad_projection = proj_total.astype(jnp.bfloat16)
    return (
        grad_queries,
        grad_keys,
        grad_values,
        grad_projection,
        grad_glu,
        kernel_total,
        gain_total,
    )


def solution(mesh):
    in_specs = (
        P("dp", "tm", None),
        P("dp", "tm", None),
        P("dp", "tm", None),
        P("dp"),
        P("dp", None),
        P("dp", "tm", None),
        P("dp", "tm", None),
        P("dp", None),
        P("dp"),
        P("dp", "tm", None),
    )
    out_specs = (
        P("dp", "tm", None),
        P("dp", "tm", None),
        P("dp", "tm", None),
        P("dp", None),
        P("dp", "tm", None),
        P("dp", None),
        P("dp"),
    )
    return jax.shard_map(
        per_device, mesh=mesh, in_specs=in_specs, out_specs=out_specs, check_vma=False
    )
```

```python
import jax
import jax.numpy as jnp
from jax import lax
from jax.sharding import PartitionSpec as P

HEADS = 2
HDIM = 128
CH = 2048
KW = 31


NEG_FILL = -1e30
NORM_EPS = 1e-05


def from_behind(block, axis, distance):
    devices = range(lax.axis_size(axis))
    route = [((i - distance) % len(devices), i) for i in devices]
    return lax.ppermute(block, axis, route)


def extended(cells, sides, width):
    for axis, dim in sides:
        count = lax.axis_size(axis)
        ends = count - 1
        head = lax.slice_in_dim(cells, 0, width, axis=dim)
        tail = lax.slice_in_dim(cells, cells.shape[dim] - width, cells.shape[dim], axis=dim)
        cells = jnp.concatenate(
            [
                lax.ppermute(tail, axis, [(i, (i + 1) % count) for i in range(ends)]),
                cells,
                lax.ppermute(head, axis, [((i + 1) % count, i) for i in range(ends)]),
            ],
            axis=dim,
        )
    return cells


def depthwise(padded, kernel_f, frame_rows):
    mixed = jnp.zeros((frame_rows, kernel_f.shape[0]), jnp.float32)
    for tap in range(kernel_f.shape[1]):
        mixed = mixed + padded[tap : tap + frame_rows].astype(jnp.float32) * kernel_f[:, tap]
    return mixed


def back_depthwise(grad_pad, kernel_f, frame_rows):
    half_width = (kernel_f.shape[1] - 1) // 2
    result = jnp.zeros((frame_rows, kernel_f.shape[0]), jnp.float32)
    for tap in range(kernel_f.shape[1]):
        begin = 2 * half_width - tap
        result = (
            result + grad_pad[begin : begin + frame_rows].astype(jnp.float32) * kernel_f[:, tap]
        )
    return result


def tap_products(grad_low, padded, frame_rows, tap_count):
    grad_f = grad_low.astype(jnp.float32)
    return jnp.stack(
        [
            jnp.sum(grad_f * padded[tap : tap + frame_rows].astype(jnp.float32), axis=0)
            for tap in range(tap_count)
        ],
        axis=1,
    )


def norm_backward(mixed, gain_f, cotangent, frame_live):
    centre = mixed - jnp.mean(mixed, axis=-1, keepdims=True)
    inv_std = lax.rsqrt(jnp.mean(centre * centre, axis=-1, keepdims=True) + NORM_EPS)
    standard = centre * inv_std
    normed = standard * gain_f
    squash = jax.nn.sigmoid(normed)
    grad_normed = (
        cotangent.astype(jnp.float32) * frame_live * (squash + normed * squash * (1.0 - squash))
    )
    gain_term = jnp.sum(grad_normed * standard, axis=0)
    scaled = grad_normed * gain_f
    grad_conv = inv_std * (
        scaled
        - jnp.mean(scaled, axis=-1, keepdims=True)
        - standard * jnp.mean(scaled * standard, axis=-1, keepdims=True)
    )
    return (grad_conv.astype(jnp.bfloat16), gain_term)


def gather_params(projection, kernel, norm_gain):
    width = projection.shape[1]
    tail = jnp.concatenate([kernel.reshape(-1), norm_gain.reshape(-1)])
    tail_rows = -(-tail.shape[0] // width)
    tail = jnp.pad(tail, (0, tail_rows * width - tail.shape[0])).reshape(tail_rows, width)
    block = jnp.concatenate([projection, tail], axis=0)
    full = lax.all_gather(block, "dp", axis=0, tiled=False)
    count = full.shape[0]
    proj_rows = projection.shape[0]
    full_proj = full[:, :proj_rows].reshape(count * proj_rows, width)
    flat_tail = full[:, proj_rows:].reshape(count, tail_rows * width)
    kernel_size = kernel.shape[0] * kernel.shape[1]
    full_kernel = flat_tail[:, :kernel_size].reshape(count * kernel.shape[0], kernel.shape[1])
    full_gain = flat_tail[:, kernel_size : kernel_size + norm_gain.shape[0]].reshape(-1)
    return full_proj, full_kernel, full_gain


def reduce_grads(proj_term, kernel_term, gain_term):
    count = lax.axis_size("dp")
    width = proj_term.shape[1]
    proj_part = lax.psum_scatter(proj_term, "dp", scatter_dimension=0, tiled=True)
    proj_part, kernel_term, gain_term = lax.optimization_barrier((proj_part, kernel_term, gain_term))
    kernel_blocks = kernel_term.reshape(count, -1)
    gain_blocks = gain_term.reshape(count, -1)
    tail = jnp.concatenate([kernel_blocks, gain_blocks], axis=1)
    tail_cols = tail.shape[1]
    tail_rows = -(-tail_cols // width)
    tail = jnp.pad(tail, ((0, 0), (0, tail_rows * width - tail_cols))).reshape(-1, width)
    tail_part = lax.psum_scatter(tail, "dp", scatter_dimension=0, tiled=True)
    total = lax.psum(jnp.concatenate([proj_part, tail_part], axis=0), "tm")
    proj_rows = proj_part.shape[0]
    proj_total = total[:proj_rows]
    flat_tail = total[proj_rows:].reshape(-1)
    kernel_size = kernel_blocks.shape[1]
    kernel_total = flat_tail[:kernel_size].reshape(-1, kernel_term.shape[1])
    gain_total = flat_tail[kernel_size : kernel_size + gain_blocks.shape[1]]
    return proj_total, kernel_total, gain_total


def gather_tm(block):
    count = lax.axis_size("tm")
    parts = [block] + [
        lax.ppermute(block, "tm", [(i, (i + k) % count) for i in range(count)])
        for k in range(1, count)
    ]
    return jnp.stack(parts)


def split_three(values):
    high = lax.optimization_barrier(values.astype(jnp.bfloat16))
    rest = values - high.astype(jnp.float32)
    middle = lax.optimization_barrier(rest.astype(jnp.bfloat16))
    low = (rest - middle.astype(jnp.float32)).astype(jnp.bfloat16)
    return jnp.concatenate([high, middle, low], axis=0)


def join_three(parts):
    third = parts.shape[0] // 3
    wide = parts.astype(jnp.float32)
    return wide[:third] + wide[third : 2 * third] + wide[2 * third :]


def per_device(
    queries,
    key_input,
    value_input,
    lengths,
    projection,
    upstream,
    glu_input,
    kernel,
    norm_gain,
    conv_upstream,
):
    time_count = lax.axis_size("tm")
    time_rank = lax.axis_index("tm")
    frame_rows = queries.shape[1]
    flat_width = queries.shape[2]
    score_scale = HDIM ** (-0.5)
    length = lengths[0]
    full_proj, full_kernel, full_gain = gather_params(projection, kernel, norm_gain)
    query_heads = queries[0].reshape(frame_rows, HEADS, HDIM)
    key_own = key_input[0].reshape(frame_rows, HEADS, HDIM)
    value_own = value_input[0].reshape(frame_rows, HEADS, HDIM)
    key_value = gather_tm(jnp.concatenate([key_input[0], value_input[0]], axis=1))
    key_source = (time_rank - jnp.arange(time_count, dtype=jnp.int32)) % time_count
    key_frames = key_source[:, None] * frame_rows + jnp.arange(frame_rows, dtype=jnp.int32)
    key_value = key_value.reshape(-1, key_value.shape[-1])
    total_frames = key_value.shape[0]
    key_all = key_value[:, :flat_width].reshape(total_frames, HEADS, HDIM)
    value_all = key_value[:, flat_width:].reshape(total_frames, HEADS, HDIM)
    key_live = key_frames.reshape(-1) < length
    scores = (
        jnp.einsum("qhd,khd->hqk", query_heads, key_all, preferred_element_type=jnp.float32)
        * score_scale
    )
    scores = jnp.where(key_live[None, None, :], scores, NEG_FILL)
    row_top = jnp.max(scores, axis=-1)
    log_total = row_top + jnp.log(jnp.sum(jnp.exp(scores - row_top[:, :, None]), axis=-1))
    weights = jnp.exp(scores - log_total[:, :, None])
    weights_high = lax.optimization_barrier(weights.astype(jnp.bfloat16))
    weights_rest = (weights - weights_high.astype(jnp.float32)).astype(jnp.bfloat16)
    attended = (
        jnp.einsum("hqk,khd->qhd", weights_high, value_all, preferred_element_type=jnp.float32)
        + jnp.einsum("hqk,khd->qhd", weights_rest, value_all, preferred_element_type=jnp.float32)
    ).astype(jnp.bfloat16)
    upstream_rows = upstream[0]
    grad_out = jnp.dot(upstream_rows, full_proj, preferred_element_type=jnp.float32).astype(
        jnp.bfloat16
    )
    grad_heads = grad_out.reshape(frame_rows, HEADS, HDIM)
    row_delta = jnp.einsum("qhd,qhd->hq", grad_heads, attended, preferred_element_type=jnp.float32)
    grad_weights = jnp.einsum(
        "qhd,khd->hqk", grad_heads, value_all, preferred_element_type=jnp.float32
    )
    grad_scores = (weights * (grad_weights - row_delta[:, :, None]) * score_scale).astype(
        jnp.bfloat16
    )
    query_acc = jnp.einsum("hqk,khd->qhd", grad_scores, key_all, preferred_element_type=jnp.float32)
    stat_parts = split_three(jnp.concatenate([log_total, row_delta], axis=0))
    pair_width = 2 * flat_width
    stat_rows = -(-stat_parts.size // pair_width)
    stat_rows = -(-stat_rows // 16) * 16
    stat_block = jnp.pad(stat_parts.reshape(-1), (0, stat_rows * pair_width - stat_parts.size))
    packed_rows = jnp.concatenate(
        [
            jnp.concatenate([queries[0], grad_out], axis=1),
            stat_block.reshape(stat_rows, pair_width),
        ],
        axis=0,
    )
    query_grad = gather_tm(packed_rows)
    query_pairs = query_grad[:, :frame_rows].reshape(total_frames, pair_width)
    stat_all = query_grad[:, frame_rows:].reshape(time_count, -1)[:, : stat_parts.size]
    stat_all = stat_all.reshape(time_count, stat_parts.shape[0], frame_rows)
    stat_all = join_three(jnp.transpose(stat_all, (1, 0, 2)).reshape(stat_parts.shape[0], -1))
    query_all = query_pairs[:, :flat_width].reshape(total_frames, HEADS, HDIM)
    grad_all = query_pairs[:, flat_width:].reshape(total_frames, HEADS, HDIM)
    log_total_all = stat_all[:HEADS]
    row_delta_all = stat_all[HEADS:]
    own_live = time_rank * frame_rows + jnp.arange(frame_rows, dtype=jnp.int32) < length
    scores_k = (
        jnp.einsum("qhd,khd->hqk", query_all, key_own, preferred_element_type=jnp.float32)
        * score_scale
    )
    scores_k = jnp.where(own_live[None, None, :], scores_k, NEG_FILL)
    weights_k = jnp.exp(scores_k - log_total_all[:, :, None])
    value_acc = jnp.einsum(
        "hqk,qhd->khd", weights_k.astype(jnp.bfloat16), grad_all, preferred_element_type=jnp.float32
    )
    grad_weights_k = jnp.einsum(
        "qhd,khd->hqk", grad_all, value_own, preferred_element_type=jnp.float32
    )
    grad_scores_k = (
        weights_k * (grad_weights_k - row_delta_all[:, :, None]) * score_scale
    ).astype(jnp.bfloat16)
    key_acc = jnp.einsum("hqk,qhd->khd", grad_scores_k, query_all, preferred_element_type=jnp.float32)
    grad_queries = query_acc.reshape(1, frame_rows, flat_width).astype(jnp.bfloat16)
    grad_keys = key_acc.reshape(1, frame_rows, flat_width).astype(jnp.bfloat16)
    grad_values = value_acc.reshape(1, frame_rows, flat_width).astype(jnp.bfloat16)
    half_width = (KW - 1) // 2
    frame_ids = time_rank * frame_rows + jnp.arange(frame_rows, dtype=jnp.int32)
    frame_live = (frame_ids < length).astype(jnp.float32)[:, None]
    glu_rows = glu_input[0]
    linear = glu_rows[:, :CH].astype(jnp.float32)
    gate_sig = jax.nn.sigmoid(glu_rows[:, CH:].astype(jnp.float32))
    activ = (linear * gate_sig * frame_live).astype(jnp.bfloat16)
    padded = extended(activ, (("tm", 0),), half_width)
    kernel_f = full_kernel.astype(jnp.float32)
    gain_f = full_gain.astype(jnp.float32)
    attended_flat = attended.reshape(frame_rows, flat_width)
    proj_term = lax.dot_general(
        upstream_rows,
        attended_flat,
        (((0,), (0,)), ((), ())),
        preferred_element_type=jnp.float32,
    )
    proj_term, padded = lax.optimization_barrier((proj_term, padded))
    mixed = depthwise(padded, kernel_f, frame_rows)
    grad_conv, gain_term = norm_backward(mixed, gain_f, conv_upstream[0], frame_live)
    grad_pad = extended(grad_conv, (("tm", 0),), half_width)
    kernel_term = tap_products(grad_conv, padded, frame_rows, KW)
    grad_activ = back_depthwise(grad_pad, kernel_f, frame_rows) * frame_live
    first_half = grad_activ * gate_sig
    second_half = grad_activ * linear * gate_sig * (1.0 - gate_sig)
    grad_glu = jnp.concatenate([first_half, second_half], axis=-1).astype(jnp.bfloat16)[None]
    proj_total, kernel_total, gain_total = reduce_grads(proj_term, kernel_term, gain_term)
    grad_projection = proj_total.astype(jnp.bfloat16)
    return (
        grad_queries,
        grad_keys,
        grad_values,
        grad_projection,
        grad_glu,
        kernel_total,
        gain_total,
    )


def solution(mesh):
    in_specs = (
        P("dp", "tm", None),
        P("dp", "tm", None),
        P("dp", "tm", None),
        P("dp"),
        P("dp", None),
        P("dp", "tm", None),
        P("dp", "tm", None),
        P("dp", None),
        P("dp"),
        P("dp", "tm", None),
    )
    out_specs = (
        P("dp", "tm", None),
        P("dp", "tm", None),
        P("dp", "tm", None),
        P("dp", None),
        P("dp", "tm", None),
        P("dp", None),
        P("dp"),
    )
    return jax.shard_map(
        per_device, mesh=mesh, in_specs=in_specs, out_specs=out_specs, check_vma=False
    )
```
